256 devices in a mesh: cell: 16 (over z, core), energy: 16 (over y, x).
Axes of the slice: x: 4, y: 4, z: 8, core: 2. Of those that a mesh axis runs over, the one named last changes fastest.
Arguments:
- ham_diag: float32 [16, 768, 768], P('cell'), as said below
- couple: float32 [16, 128, 128], P('cell'), as said below
- couple_mask: int32 [16, 2, 2], P('cell'), may hold values from 0 to 1, as said below
- energies: float32 [16], P('energy'), may hold values from -0.02 to 0
- lead_front: float32 [16, 128, 128], P('energy'), as said below
- block_list: int32 [16, 16, 2], P('cell'), may hold values from 0 to 11, as said below
- derivative: float32 [16, 16, 4096], P('cell', 'energy'), may hold values from -0.24 to 0.24
- pair_list: int32 [16, 2], replicated, may hold values from 0 to 15
Outputs:
- local_density: float32 [16, 12288], P('energy', 'cell')
- phonon_self: float32 [16, 16, 16, 4096], P('cell', 'energy')
The draws below stay inside these ranges and needn't reach their ends.
Inputs may be any that keep to these rules, and one draw needn't show every extreme that they name: Each block is symmetric with diagonal entries between 0.1 and 1.5. For every energy in the range of energies, the block-tridiagonal matrix with diagonal blocks ham_diag[c] - energy I and the masked couplings between cells, with coupled[0] lead_front[e] coupled[0]^T subtracted on the first 128 orbitals of cell 0, is positive definite, so that every shifted block, front and reduced matrix is positive definite. `couple`: with its own cell's couple_mask applied, each coupling has spectral norm at most 0.5. `lead_front`: each matrix is symmetric and positive definite with spectral norm at most 1.7, its diagonal entries in 0.5 to 1.5. `block_list`: entry 0 is the block row and entry 1 the block column of a listed 64-block of the cell; about half of the listed blocks are diagonal blocks. `couple_mask`: 1 keeps a block of the coupling, 0 removes it; the diagonal blocks of every cell are kept. `pair_list`: entry 0 names the energy of the first Green's function block, entry 1 that of the second.
All inputs are finite; a program needn't handle non-finite values.
Results may differ from the reference program's by a relative error of at most 0.0003.
Values sent between devices are 32-bit elements; how exact they have to be, the bound alone decides.
No kernel may reach another device: no remote copies, remote signals or barrier semaphores. Data moves between devices by JAX's collectives and lax.ppermute only.
A program may use at most 64 MiB of HBM per device.

```python
import math
import jax
import jax.numpy as jnp
from jax import lax

B = 768
SURF = 128
BLK = 64
PAIRS = 16
NBLK = 12
CELLS = 16
ENERGIES = 16
NB = 16


def spectral_norm(matrix):
    gram_matrix = jnp.einsum('cij,cik->cjk', matrix, matrix, precision=lax.Precision.HIGHEST)
    return jnp.sqrt(jnp.max(jnp.linalg.eigvalsh(gram_matrix), axis=-1))


def symmetric_part(key, count_mats, mat_width, target_norm):
    raw_values = jax.random.normal(key, (count_mats, mat_width, mat_width), jnp.float32)
    identity = jnp.eye(mat_width, dtype=jnp.float32)
    symmetric = (raw_values + jnp.swapaxes(raw_values, 1, 2)) * (1.0 - identity)
    largest = jnp.max(jnp.abs(jnp.linalg.eigvalsh(symmetric)), axis=-1)
    return symmetric * (target_norm / largest)[:, None, None]


def orthogonal(key, count_mats, mat_width):
    vectors = jax.random.normal(key, (count_mats, mat_width, mat_width), jnp.float32)
    identity_stack = jnp.broadcast_to(jnp.eye(mat_width, dtype=jnp.float32), (count_mats, mat_width, mat_width))

    def reflect(step_index, current):
        vector = lax.dynamic_index_in_dim(vectors, step_index, 1, keepdims=False)
        reflect_scale = 2.0 / jnp.sum(vector * vector, axis=-1)
        image_vec = jnp.einsum('cij,cj->ci', current, vector, precision=lax.Precision.HIGHEST)
        return current - reflect_scale[:, None, None] * image_vec[:, :, None] * vector[:, None, :]
    return lax.fori_loop(0, mat_width, reflect, identity_stack)


def draw_ham_diag(key, part):
    inner_size = B - 2 * SURF
    key_rough = jax.random.fold_in(key, 11)
    key_link = jax.random.fold_in(key, 12)
    key_cell = jax.random.fold_in(key, 16)
    key_bond = jax.random.fold_in(key, 17)
    rough_part = jax.random.uniform(key_rough, (CELLS, 2 * SURF), jnp.float32, 0.0, 1.0)
    cell_draw = jax.random.uniform(key_cell, (CELLS, 1), jnp.float32, 0.0, 1.0)
    bond_draw = jax.random.uniform(key_bond, (CELLS,), jnp.float32, 0.0, 1.0)
    cell_term = cell_draw * cell_draw
    intra_strength = 0.35 + 0.15 * bond_draw
    excess = 0.0025 + 0.009 * cell_term + 0.002 * rough_part
    surface_diag = 0.5 + intra_strength[:, None] + excess
    surface_eye = jnp.eye(SURF, dtype=jnp.float32)
    link_block = -intra_strength[:, None, None] * orthogonal(key_link, CELLS, SURF)
    matrix = jnp.zeros((CELLS, B, B), jnp.float32)
    matrix = matrix.at[:, :SURF, :SURF].set(surface_diag[:, :SURF, None] * surface_eye)
    matrix = matrix.at[:, B - SURF:, B - SURF:].set(surface_diag[:, SURF:, None] * surface_eye)
    matrix = matrix.at[:, :SURF, B - SURF:].set(link_block)
    matrix = matrix.at[:, B - SURF:, :SURF].set(jnp.swapaxes(link_block, 1, 2))
    if inner_size > 0:
        key_inner = jax.random.fold_in(key, 13)
        key_level = jax.random.fold_in(key, 14)
        key_edge = jax.random.fold_in(key, 15)
        inner_eye = jnp.eye(inner_size, dtype=jnp.float32)
        level_draw = jax.random.uniform(key_level, (CELLS, inner_size), jnp.float32, 0.0, 1.0)
        level_part = 0.1 * jnp.exp(math.log(15.0) * level_draw)
        inner_block = symmetric_part(key_inner, CELLS, inner_size, 0.04) + level_part[:, :, None] * inner_eye
        edge_links = jax.random.normal(key_edge, (CELLS, 2, inner_size, SURF), jnp.float32)
        edge_first = edge_links[:, 0]
        edge_last = edge_links[:, 1]
        edge_first = edge_first * (0.004 / spectral_norm(edge_first))[:, None, None]
        edge_last = edge_last * (0.004 / spectral_norm(edge_last))[:, None, None]
        matrix = matrix.at[:, SURF:B - SURF, SURF:B - SURF].set(inner_block)
        matrix = matrix.at[:, SURF:B - SURF, :SURF].set(edge_first)
        matrix = matrix.at[:, :SURF, SURF:B - SURF].set(jnp.swapaxes(edge_first, 1, 2))
        matrix = matrix.at[:, SURF:B - SURF, B - SURF:].set(edge_last)
        matrix = matrix.at[:, B - SURF:, SURF:B - SURF].set(jnp.swapaxes(edge_last, 1, 2))
    return matrix


def mask_levels(key):
    key_mask = jax.random.fold_in(key, 51)
    return jax.random.randint(key_mask, (CELLS, SURF // BLK, SURF // BLK), 0, 4, dtype=jnp.int32)


def mask_from(levels):
    kept_blocks = jnp.minimum(levels, 1)
    diagonal = jnp.eye(SURF // BLK, dtype=jnp.int32)[None]
    return jnp.maximum(kept_blocks, diagonal)


def draw_couple_mask(key, part):
    return mask_from(mask_levels(key))


def draw_couple(key, part):
    key_first = jax.random.fold_in(key, 41)
    key_second = jax.random.fold_in(key, 42)
    key_mixing = jax.random.fold_in(key, 43)
    first_block = orthogonal(key_first, CELLS, BLK)
    second_block = orthogonal(key_second, CELLS, BLK)
    mixing = orthogonal(key_mixing, CELLS, BLK)
    mix_sine = 0.25
    mix_cosine = math.sqrt(1.0 - mix_sine * mix_sine)
    high = lax.Precision.HIGHEST
    upper_right = -mix_sine * jnp.einsum('cij,cjk->cik', first_block, mixing, precision=high)
    lower_left = mix_sine * jnp.einsum('cij,ckj->cik', second_block, mixing, precision=high)
    upper_rows = jnp.concatenate([mix_cosine * first_block, upper_right], axis=2)
    lower_rows = jnp.concatenate([lower_left, mix_cosine * second_block], axis=2)
    rotation = jnp.concatenate([upper_rows, lower_rows], axis=1)
    mask_blocks = mask_from(mask_levels(key)).astype(jnp.float32)
    mask_width = SURF // BLK
    expanded = jnp.broadcast_to(mask_blocks[:, :, None, :, None], (CELLS, mask_width, BLK, mask_width, BLK)).reshape(CELLS, SURF, SURF)
    masked = rotation * expanded
    norms = spectral_norm(masked)
    return rotation * (0.5 / norms)[:, None, None]


def draw_lead_front(key, part):
    key_off = jax.random.fold_in(key, 21)
    key_diag = jax.random.fold_in(key, 22)
    offdiag = symmetric_part(key_off, ENERGIES, SURF, 0.2)
    diagonal = jax.random.uniform(key_diag, (ENERGIES, SURF), jnp.float32, 0.5, 1.5)
    identity = jnp.eye(SURF, dtype=jnp.float32)
    return offdiag + diagonal[:, :, None] * identity


def draw_block_list(key, part):
    key_row = jax.random.fold_in(key, 31)
    key_other = jax.random.fold_in(key, 32)
    key_same = jax.random.fold_in(key, 33)
    row_blocks = jax.random.randint(key_row, (CELLS, NB), 0, NBLK, dtype=jnp.int32)
    other_blocks = jax.random.randint(key_other, (CELLS, NB), 0, NBLK, dtype=jnp.int32)
    same_flag = jax.random.randint(key_same, (CELLS, NB), 0, 2, dtype=jnp.int32)
    column_blocks = jnp.where(same_flag == 1, row_blocks, other_blocks)
    return jnp.stack([row_blocks, column_blocks], axis=-1)


def plant(array, key, low, high):
    longest = array.shape.index(max(array.shape))
    spots = []
    for shift in (0, 1):
        where = [jax.random.randint(jax.random.fold_in(key, axis), (), 0, length) for axis, length in enumerate(array.shape)]
        where[longest] = (where[longest] + shift) % array.shape[longest]
        spots.append(tuple(where))
    return array.at[spots[0]].set(low).at[spots[1]].set(high)


def block_scale(own_key, extent, cuts, smallest, high):
    loudness = 1.0
    for dim, parts in cuts:
        heights = jax.random.uniform(jax.random.fold_in(jax.random.fold_in(own_key, 6), dim), (parts,), jnp.float32, smallest / len(cuts), high / len(cuts))
        loudness = loudness * jnp.repeat(jnp.exp(heights), extent[dim] // parts).reshape((-1,) + (1,) * (len(extent) - 1 - dim))
    return loudness


def bell_draw(key, extent, width, limit, cuts=(), held_as=jnp.bfloat16):
    values = width * jax.random.normal(key, extent, jnp.float32)
    if cuts:
        values = values * block_scale(key, extent, cuts, -0.22, 0.18)
    return jnp.clip(values, -limit, limit).astype(held_as)


def setup_inputs(seed: int = 0) -> dict:
    keys = jax.random.split(jax.random.key(seed), 9)
    return {
        "ham_diag": draw_ham_diag(jax.random.fold_in(keys[8], 71), 0),
        "couple": draw_couple(jax.random.fold_in(keys[8], 71), 0),
        "couple_mask": draw_couple_mask(jax.random.fold_in(keys[8], 71), 0),
        "energies": jnp.clip(-0.02 + 0.02 * jax.random.uniform(keys[3], (ENERGIES,), jnp.float32) ** block_scale(keys[3], (ENERGIES,), ((0, 16),), -0.2, 0.2), -0.02, 0.0),
        "lead_front": draw_lead_front(jax.random.fold_in(keys[8], 71), 0),
        "block_list": draw_block_list(jax.random.fold_in(keys[8], 71), 0),
        "derivative": bell_draw(keys[6], (CELLS, NB, BLK * BLK), 0.04, 0.24, ((0, 16), (1, 16)), jnp.float32),
        "pair_list": plant(jax.random.randint(keys[7], (PAIRS, 2), 0, ENERGIES), jax.random.fold_in(keys[7], 1), 0, ENERGIES - 1).astype(jnp.int32),
    }


def matmul(left_side, right_side):
    return jnp.matmul(left_side, right_side, precision=lax.Precision.HIGHEST)

def invert(matrix):
    lower_factor = jnp.linalg.cholesky(matrix)
    identity = jnp.eye(matrix.shape[-1], dtype=matrix.dtype)
    return jax.scipy.linalg.cho_solve((lower_factor, True), identity)

def expand_mask(couple, couple_mask):
    cell_count = couple.shape[0]
    mask_width = couple_mask.shape[1]
    shaped = couple.reshape(cell_count, mask_width, BLK, mask_width, BLK)
    return (shaped * couple_mask[:, :, None, :, None].astype(couple.dtype)).reshape(couple.shape)

def self_energy(regrouped, derivative, pair_list):
    first_pick = jnp.take(regrouped, pair_list[:, 0], axis=0)
    second_pick = jnp.take(regrouped, pair_list[:, 1], axis=0)
    pair_count = pair_list.shape[0]
    listed = derivative.shape[0]
    first_pick = first_pick.reshape(pair_count, listed, BLK, BLK)
    second_pick = second_pick.reshape(pair_count, listed, BLK, BLK)
    coupling_mat = derivative.reshape(listed, BLK, BLK)
    high = lax.Precision.HIGHEST
    left_side = jnp.einsum('nij,pnjk->pnik', coupling_mat, first_pick, precision=high)
    left_side = jnp.einsum('pnik,nlk->pnil', left_side, coupling_mat, precision=high)
    result = jnp.einsum('pnil,pnml->npim', left_side, second_pick, precision=high)
    return result.reshape(listed, pair_count, BLK * BLK)

def reference(ham_diag, couple, couple_mask, energies, lead_front, block_list, derivative, pair_list):
    coupled = expand_mask(couple, couple_mask)
    identity = jnp.eye(B, dtype=ham_diag.dtype)
    surface_eye = jnp.eye(SURF, dtype=ham_diag.dtype)
    row_blocks = block_list[:, :, 0]
    column_blocks = block_list[:, :, 1]

    def one_energy(inputs):
        energy, lead_green = inputs

        def forward(previous, pieces):
            hamiltonian, coupling = pieces
            inverses = invert(hamiltonian - energy * identity)
            factor = matmul(coupling, jnp.linalg.cholesky(previous))
            reduced = surface_eye - matmul(factor.T, matmul(inverses[:SURF, :SURF], factor))
            root_reduced = jnp.linalg.cholesky(reduced)
            left_cols = matmul(inverses[:, :SURF], factor)
            solved = jax.scipy.linalg.cho_solve((root_reduced, True), left_cols.T)
            green = inverses + matmul(left_cols, solved)
            return (green[B - SURF:, B - SURF:], green)
        last_front, greens = lax.scan(forward, lead_green, (ham_diag, coupled))

        def backward(weight, pieces):
            green, coupling, rows_here, columns_here = pieces
            green_full = green + matmul(matmul(green[:, B - SURF:], weight), green[B - SURF:, :])
            weight_next = matmul(matmul(coupling.T, green_full[:SURF, :SURF]), coupling)
            blocks = green_full.reshape(NBLK, BLK, NBLK, BLK)[rows_here, :, columns_here, :]
            return (weight_next, (jnp.diagonal(green_full), blocks.reshape(NB, BLK * BLK)))
        start_weight = jnp.zeros((SURF, SURF), dtype=ham_diag.dtype)
        unused, outputs = lax.scan(backward, start_weight, (greens, coupled, row_blocks, column_blocks), reverse=True)
        diagonal, blocks = outputs
        return (diagonal.reshape(CELLS * B), blocks)
    local_density, picked = lax.map(one_energy, (energies, lead_front))

    def cell_energy(pieces):
        picked_cell, derivative_cell = pieces
        return self_energy(picked_cell, derivative_cell, pair_list)
    phonon_self = lax.map(cell_energy, (jnp.swapaxes(picked, 0, 1), derivative))
    return (local_density, phonon_self)
```

```python
import jax
import jax.numpy as jnp
from jax import lax
from jax.sharding import PartitionSpec as P

BLK = 64


def passed_along(value, axis, steps):
    count = lax.axis_size(axis)
    first, last = (max(0, -steps), min(count, count - steps))
    return lax.ppermute(value, axis, [(source, source + steps) for source in range(first, last)])


def matmul(left_side, right_side):
    return jnp.matmul(left_side, right_side, precision=lax.Precision.HIGHEST)


def tmat(matrix):
    return jnp.swapaxes(matrix, -1, -2)


def invert(matrix):
    lower_factor = jnp.linalg.cholesky(matrix)
    identity = jnp.eye(matrix.shape[-1], dtype=matrix.dtype)
    return jax.scipy.linalg.cho_solve((lower_factor, True), identity)


def lower_solve(lower_factor, rhs):
    return jax.scipy.linalg.solve_triangular(lower_factor, rhs, lower=True)


def expand_mask(couple, couple_mask):
    cell_count = couple.shape[0]
    mask_width = couple_mask.shape[1]
    shaped = couple.reshape(cell_count, mask_width, BLK, mask_width, BLK)
    return (shaped * couple_mask[:, :, None, :, None].astype(couple.dtype)).reshape(couple.shape)


def combine(left_seg, right_seg):
    p_a, q_a, r_a = left_seg
    p_b, q_b, r_b = right_seg
    surface = r_a.shape[-1]
    eye = jnp.eye(surface, dtype=r_a.dtype)
    root = jnp.linalg.cholesky(r_a)
    root_t = tmat(root)
    lp = matmul(root_t, p_b)
    reduced = eye - matmul(lp, root)
    root_reduced = jnp.linalg.cholesky(reduced)
    rhs = jnp.concatenate([matmul(root_t, q_b), matmul(lp, tmat(q_a))], axis=-1)
    solved = lower_solve(root_reduced, rhs)
    gram = matmul(tmat(solved), solved)
    r_c = r_b + gram[..., :surface, :surface]
    q_c = matmul(q_a, q_b) + gram[..., surface:, :surface]
    p_c = p_a + matmul(matmul(q_a, p_b), tmat(q_a)) + gram[..., surface:, surface:]
    return (p_c, q_c, r_c)


def self_energy(regrouped, derivative, pair_list):
    first_pick = jnp.take(regrouped, pair_list[:, 0], axis=0)
    second_pick = jnp.take(regrouped, pair_list[:, 1], axis=0)
    pair_count = pair_list.shape[0]
    listed = derivative.shape[0]
    first_pick = first_pick.reshape(pair_count, listed, BLK, BLK)
    second_pick = second_pick.reshape(pair_count, listed, BLK, BLK)
    coupling_mat = derivative.reshape(listed, BLK, BLK)
    high = lax.Precision.HIGHEST
    left_side = jnp.einsum("nij,pnjk->pnik", coupling_mat, first_pick, precision=high)
    left_side = jnp.einsum("pnik,nlk->pnil", left_side, coupling_mat, precision=high)
    result = jnp.einsum("pnil,pnml->npim", left_side, second_pick, precision=high)
    return result.reshape(listed, pair_count, BLK * BLK)


def on_device(
    ham_diag, couple, couple_mask, energies, lead_front, block_list, derivative, pair_list
):
    cell_count = lax.axis_size("cell")
    cell_index = lax.axis_index("cell")
    surface = couple.shape[1]
    size = ham_diag.shape[1]
    coupling = expand_mask(couple, couple_mask)[0]
    eye = jnp.eye(surface, dtype=jnp.float32)
    is_first = cell_index == 0
    is_last = cell_index == cell_count - 1

    lead_self = matmul(matmul(coupling, lead_front[0]), coupling.T)
    lead_self = jnp.where(is_first, lead_self, jnp.zeros_like(lead_self))
    shifted = ham_diag[0] - energies[0] * jnp.eye(size, dtype=jnp.float32)
    shifted = shifted.at[:surface, :surface].add(-lead_self)
    inverse = invert(shifted)

    corner = inverse[:surface, :surface]
    leaf = (
        matmul(matmul(coupling.T, corner), coupling),
        matmul(coupling.T, inverse[:surface, -surface:]),
        inverse[-surface:, -surface:],
    )
    prefix = leaf
    suffix = leaf
    distance = 1
    while distance < cell_count:
        from_left = passed_along(prefix, "cell", distance)
        from_right = passed_along(suffix, "cell", -distance)
        has_left = cell_index >= distance
        has_right = cell_index + distance < cell_count
        safe_left = jnp.where(has_left, from_left[2], eye)
        left_segs = tuple(
            jnp.stack([a, b]) for a, b in zip((from_left[0], from_left[1], safe_left), suffix)
        )
        right_segs = tuple(jnp.stack([a, b]) for a, b in zip(prefix, from_right))
        joined = combine(left_segs, right_segs)
        prefix = tuple(jnp.where(has_left, j[0], o) for j, o in zip(joined, prefix))
        suffix = tuple(jnp.where(has_right, j[1], o) for j, o in zip(joined, suffix))
        distance *= 2

    front_before = passed_along(prefix[2], "cell", 1)
    right_self = passed_along(suffix[0], "cell", -1)
    front_before = jnp.where(is_first, eye, front_before)
    right_self = jnp.where(is_last, jnp.zeros_like(right_self), right_self)

    roots = jnp.linalg.cholesky(jnp.stack([front_before, prefix[2]]))
    factor = matmul(coupling, roots[0])
    factor = jnp.where(is_first, jnp.zeros_like(factor), factor)
    root_front = roots[1]
    reduced_left = eye - matmul(matmul(factor.T, corner), factor)
    reduced_right = eye - matmul(matmul(root_front.T, right_self), root_front)
    root_reduced = jnp.linalg.cholesky(jnp.stack([reduced_left, reduced_right]))
    left_cols = matmul(inverse[:, :surface], factor)
    solved_left = lower_solve(root_reduced[0], left_cols.T)
    green = inverse + matmul(solved_left.T, solved_left)
    edge_rows = green[-surface:, :]
    weighted_rows = matmul(right_self, edge_rows)
    solved_right = lower_solve(root_reduced[1], matmul(root_front.T, weighted_rows))
    full = green + matmul(edge_rows.T, weighted_rows) + matmul(solved_right.T, solved_right)

    local_density = jnp.diagonal(full)[None]
    block_count = size // BLK
    picked = full.reshape(block_count, BLK, block_count, BLK)[
        block_list[0, :, 0], :, block_list[0, :, 1], :
    ]
    picked = picked.reshape(1, block_list.shape[1], BLK * BLK)
    regrouped = lax.all_to_all(picked, "energy", split_axis=1, concat_axis=0, tiled=True)
    result = self_energy(regrouped, derivative[0], pair_list)
    return (local_density, result[None])


def solution(mesh):
    placed = (
        P("cell", None, None),
        P("cell", None, None),
        P("cell", None, None),
        P("energy"),
        P("energy", None, None),
        P("cell", None, None),
        P("cell", "energy", None),
        P(),
    )
    return jax.shard_map(
        on_device,
        mesh=mesh,
        in_specs=placed,
        out_specs=(P("energy", "cell"), P("cell", "energy", None, None)),
        check_vma=False,
    )
```

```python
import jax
import jax.numpy as jnp
from jax import lax
from jax.sharding import PartitionSpec as P

BLK = 64


def passed_along(value, axis, steps):
    count = lax.axis_size(axis)
    first, last = (max(0, -steps), min(count, count - steps))
    return lax.ppermute(value, axis, [(source, source + steps) for source in range(first, last)])


def matmul(left_side, right_side):
    return jnp.matmul(left_side, right_side, precision=lax.Precision.HIGHEST)


def tmat(matrix):
    return jnp.swapaxes(matrix, -1, -2)


def invert(matrix):
    lower_factor = jnp.linalg.cholesky(matrix)
    identity = jnp.eye(matrix.shape[-1], dtype=matrix.dtype)
    lower_inverse = jax.scipy.linalg.solve_triangular(lower_factor, identity, lower=True)
    return matmul(lower_inverse.T, lower_inverse)


def lower_solve(lower_factor, rhs):
    return jax.scipy.linalg.solve_triangular(lower_factor, rhs, lower=True)


def expand_mask(couple, couple_mask):
    cell_count = couple.shape[0]
    mask_width = couple_mask.shape[1]
    shaped = couple.reshape(cell_count, mask_width, BLK, mask_width, BLK)
    return (shaped * couple_mask[:, :, None, :, None].astype(couple.dtype)).reshape(couple.shape)


def combine(left_seg, right_seg):
    p_a, q_a, r_a = left_seg
    p_b, q_b, r_b = right_seg
    surface = r_a.shape[-1]
    eye = jnp.eye(surface, dtype=r_a.dtype)
    root = jnp.linalg.cholesky(r_a)
    root_t = tmat(root)
    lp = matmul(root_t, p_b)
    reduced = eye - matmul(lp, root)
    root_reduced = jnp.linalg.cholesky(reduced)
    rhs = jnp.concatenate([matmul(root_t, q_b), matmul(lp, tmat(q_a))], axis=-1)
    solved = lower_solve(root_reduced, rhs)
    gram = matmul(tmat(solved), solved)
    r_c = r_b + gram[..., :surface, :surface]
    q_c = matmul(q_a, q_b) + gram[..., surface:, :surface]
    p_c = p_a + matmul(matmul(q_a, p_b), tmat(q_a)) + gram[..., surface:, surface:]
    return (p_c, q_c, r_c)


def self_energy(regrouped, derivative, pair_list):
    first_pick = jnp.take(regrouped, pair_list[:, 0], axis=0)
    second_pick = jnp.take(regrouped, pair_list[:, 1], axis=0)
    pair_count = pair_list.shape[0]
    listed = derivative.shape[0]
    first_pick = first_pick.reshape(pair_count, listed, BLK, BLK)
    second_pick = second_pick.reshape(pair_count, listed, BLK, BLK)
    coupling_mat = derivative.reshape(listed, BLK, BLK)
    high = lax.Precision.HIGHEST
    left_side = jnp.einsum("nij,pnjk->pnik", coupling_mat, first_pick, precision=high)
    left_side = jnp.einsum("pnik,nlk->pnil", left_side, coupling_mat, precision=high)
    result = jnp.einsum("pnil,pnml->npim", left_side, second_pick, precision=high)
    return result.reshape(listed, pair_count, BLK * BLK)


def on_device(
    ham_diag, couple, couple_mask, energies, lead_front, block_list, derivative, pair_list
):
    cell_count = lax.axis_size("cell")
    cell_index = lax.axis_index("cell")
    surface = couple.shape[1]
    size = ham_diag.shape[1]
    coupling = expand_mask(couple, couple_mask)[0]
    eye = jnp.eye(surface, dtype=jnp.float32)
    is_first = cell_index == 0
    is_last = cell_index == cell_count - 1

    lead_self = matmul(matmul(coupling, lead_front[0]), coupling.T)
    lead_self = jnp.where(is_first, lead_self, jnp.zeros_like(lead_self))
    shifted = ham_diag[0] - energies[0] * jnp.eye(size, dtype=jnp.float32)
    shifted = shifted.at[:surface, :surface].add(-lead_self)
    inverse = invert(shifted)

    corner = inverse[:surface, :surface]
    leaf = (
        matmul(matmul(coupling.T, corner), coupling),
        matmul(coupling.T, inverse[:surface, -surface:]),
        inverse[-surface:, -surface:],
    )
    prefix = leaf
    distance = 1
    while distance < cell_count:
        from_left = passed_along(prefix, "cell", distance)
        has_left = cell_index >= distance
        safe_left = (from_left[0], from_left[1], jnp.where(has_left, from_left[2], eye))
        joined = combine(safe_left, prefix)
        prefix = tuple(jnp.where(has_left, j, o) for j, o in zip(joined, prefix))
        distance *= 2

    front_before = passed_along(prefix[2], "cell", 1)
    front_before = jnp.where(is_first, eye, front_before)
    factor = matmul(coupling, jnp.linalg.cholesky(front_before))
    factor = jnp.where(is_first, jnp.zeros_like(factor), factor)
    reduced = eye - matmul(matmul(factor.T, corner), factor)
    root_reduced = jnp.linalg.cholesky(reduced)
    left_cols = matmul(inverse[:, :surface], factor)
    solved = lower_solve(root_reduced, left_cols.T)
    green = inverse + matmul(solved.T, solved)

    edge_rows = green[-surface:, :]
    step_b = matmul(coupling.T, green[:surface, -surface:])
    step_a = matmul(matmul(coupling.T, green[:surface, :surface]), coupling)
    distance = 1
    while distance < cell_count:
        far_a, far_b = passed_along((step_a, step_b), "cell", -distance)
        step_a = step_a + matmul(matmul(step_b, far_a), step_b.T)
        step_b = matmul(step_b, far_b)
        distance *= 2
    weights = passed_along(step_a, "cell", -1)
    weights = jnp.where(is_last, jnp.zeros_like(weights), weights)
    full = green + matmul(edge_rows.T, matmul(weights, edge_rows))

    local_density = jnp.diagonal(full)[None]
    block_count = size // BLK
    picked = full.reshape(block_count, BLK, block_count, BLK)[
        block_list[0, :, 0], :, block_list[0, :, 1], :
    ]
    picked = picked.reshape(1, block_list.shape[1], BLK * BLK)
    regrouped = lax.all_to_all(picked, "energy", split_axis=1, concat_axis=0, tiled=True)
    result = self_energy(regrouped, derivative[0], pair_list)
    return (local_density, result[None])


def solution(mesh):
    placed = (
        P("cell", None, None),
        P("cell", None, None),
        P("cell", None, None),
        P("energy"),
        P("energy", None, None),
        P("cell", None, None),
        P("cell", "energy", None),
        P(),
    )
    return jax.shard_map(
        on_device,
        mesh=mesh,
        in_specs=placed,
        out_specs=(P("energy", "cell"), P("cell", "energy", None, None)),
        check_vma=False,
    )
```

```python
import jax
import jax.numpy as jnp
from jax import lax
from jax.sharding import PartitionSpec as P

BLK = 64


def passed_along(value, axis, steps):
    count = lax.axis_size(axis)
    first, last = (max(0, -steps), min(count, count - steps))
    return lax.ppermute(value, axis, [(source, source + steps) for source in range(first, last)])


def matmul(left_side, right_side):
    return jnp.matmul(left_side, right_side, precision=lax.Precision.HIGHEST)


def tmat(matrix):
    return jnp.swapaxes(matrix, -1, -2)


def invert_small(matrix):
    lower_factor = jnp.linalg.cholesky(matrix)
    identity = jnp.eye(matrix.shape[-1], dtype=matrix.dtype)
    lower_inverse = jax.scipy.linalg.solve_triangular(lower_factor, identity, lower=True)
    return matmul(lower_inverse.T, lower_inverse)


def invert(matrix, width=128):
    for start in range(0, matrix.shape[0], width):
        span = slice(start, start + width)
        column = matrix[:, span]
        pivot = invert_small(matrix[span, span])
        scaled = matmul(column, pivot)
        matrix = matrix - matmul(scaled, column.T)
        scaled = scaled.at[span].set(-pivot)
        matrix = matrix.at[:, span].set(scaled).at[span, :].set(scaled.T)
    return -matrix


def lower_solve(lower_factor, rhs):
    return jax.scipy.linalg.solve_triangular(lower_factor, rhs, lower=True)


def expand_mask(couple, couple_mask):
    cell_count = couple.shape[0]
    mask_width = couple_mask.shape[1]
    shaped = couple.reshape(cell_count, mask_width, BLK, mask_width, BLK)
    return (shaped * couple_mask[:, :, None, :, None].astype(couple.dtype)).reshape(couple.shape)


def combine(left_seg, right_seg):
    p_a, q_a, r_a = left_seg
    p_b, q_b, r_b = right_seg
    surface = r_a.shape[-1]
    eye = jnp.eye(surface, dtype=r_a.dtype)
    root = jnp.linalg.cholesky(r_a)
    root_t = tmat(root)
    lp = matmul(root_t, p_b)
    reduced = eye - matmul(lp, root)
    root_reduced = jnp.linalg.cholesky(reduced)
    rhs = jnp.concatenate([matmul(root_t, q_b), matmul(lp, tmat(q_a))], axis=-1)
    solved = lower_solve(root_reduced, rhs)
    gram = matmul(tmat(solved), solved)
    r_c = r_b + gram[..., :surface, :surface]
    q_c = matmul(q_a, q_b) + gram[..., surface:, :surface]
    p_c = p_a + matmul(matmul(q_a, p_b), tmat(q_a)) + gram[..., surface:, surface:]
    return (p_c, q_c, r_c)


def self_energy(regrouped, derivative, pair_list):
    first_pick = jnp.take(regrouped, pair_list[:, 0], axis=0)
    second_pick = jnp.take(regrouped, pair_list[:, 1], axis=0)
    pair_count = pair_list.shape[0]
    listed = derivative.shape[0]
    first_pick = first_pick.reshape(pair_count, listed, BLK, BLK)
    second_pick = second_pick.reshape(pair_count, listed, BLK, BLK)
    coupling_mat = derivative.reshape(listed, BLK, BLK)
    high = lax.Precision.HIGHEST
    left_side = jnp.einsum("nij,pnjk->pnik", coupling_mat, first_pick, precision=high)
    left_side = jnp.einsum("pnik,nlk->pnil", left_side, coupling_mat, precision=high)
    result = jnp.einsum("pnil,pnml->npim", left_side, second_pick, precision=high)
    return result.reshape(listed, pair_count, BLK * BLK)


def on_device(
    ham_diag, couple, couple_mask, energies, lead_front, block_list, derivative, pair_list
):
    cell_count = lax.axis_size("cell")
    cell_index = lax.axis_index("cell")
    surface = couple.shape[1]
    size = ham_diag.shape[1]
    coupling = expand_mask(couple, couple_mask)[0]
    eye = jnp.eye(surface, dtype=jnp.float32)
    is_first = cell_index == 0
    is_last = cell_index == cell_count - 1

    lead_self = matmul(matmul(coupling, lead_front[0]), coupling.T)
    lead_self = jnp.where(is_first, lead_self, jnp.zeros_like(lead_self))
    shifted = ham_diag[0] - energies[0] * jnp.eye(size, dtype=jnp.float32)
    shifted = shifted.at[:surface, :surface].add(-lead_self)
    inverse = invert(shifted)

    corner = inverse[:surface, :surface]
    leaf = (
        matmul(matmul(coupling.T, corner), coupling),
        matmul(coupling.T, inverse[:surface, -surface:]),
        inverse[-surface:, -surface:],
    )
    prefix = leaf
    distance = 1
    while distance < cell_count:
        from_left = passed_along(prefix, "cell", distance)
        has_left = cell_index >= distance
        safe_left = (from_left[0], from_left[1], jnp.where(has_left, from_left[2], eye))
        joined = combine(safe_left, prefix)
        prefix = tuple(jnp.where(has_left, j, o) for j, o in zip(joined, prefix))
        distance *= 2

    front_before = passed_along(prefix[2], "cell", 1)
    front_before = jnp.where(is_first, eye, front_before)
    factor = matmul(coupling, jnp.linalg.cholesky(front_before))
    factor = jnp.where(is_first, jnp.zeros_like(factor), factor)
    reduced = eye - matmul(matmul(factor.T, corner), factor)
    root_reduced = jnp.linalg.cholesky(reduced)
    left_cols = matmul(inverse[:, :surface], factor)
    solved = lower_solve(root_reduced, left_cols.T)
    green = inverse + matmul(solved.T, solved)

    edge_rows = green[-surface:, :]
    step_b = matmul(coupling.T, green[:surface, -surface:])
    step_a = matmul(matmul(coupling.T, green[:surface, :surface]), coupling)
    distance = 1
    while distance < cell_count:
        far_a, far_b = passed_along((step_a, step_b), "cell", -distance)
        step_a = step_a + matmul(matmul(step_b, far_a), step_b.T)
        step_b = matmul(step_b, far_b)
        distance *= 2
    weights = passed_along(step_a, "cell", -1)
    weights = jnp.where(is_last, jnp.zeros_like(weights), weights)
    full = green + matmul(edge_rows.T, matmul(weights, edge_rows))

    local_density = jnp.diagonal(full)[None]
    block_count = size // BLK
    picked = full.reshape(block_count, BLK, block_count, BLK)[
        block_list[0, :, 0], :, block_list[0, :, 1], :
    ]
    picked = picked.reshape(1, block_list.shape[1], BLK * BLK)
    regrouped = lax.all_to_all(picked, "energy", split_axis=1, concat_axis=0, tiled=True)
    result = self_energy(regrouped, derivative[0], pair_list)
    return (local_density, result[None])


def solution(mesh):
    placed = (
        P("cell", None, None),
        P("cell", None, None),
        P("cell", None, None),
        P("energy"),
        P("energy", None, None),
        P("cell", None, None),
        P("cell", "energy", None),
        P(),
    )
    return jax.shard_map(
        on_device,
        mesh=mesh,
        in_specs=placed,
        out_specs=(P("energy", "cell"), P("cell", "energy", None, None)),
        check_vma=False,
    )
```

```python
import jax
import jax.numpy as jnp
from jax import lax
from jax.sharding import PartitionSpec as P

BLK = 64


def passed_along(value, axis, steps):
    count = lax.axis_size(axis)
    first, last = (max(0, -steps), min(count, count - steps))
    return lax.ppermute(value, axis, [(source, source + steps) for source in range(first, last)])


def matmul(left_side, right_side):
    return jnp.matmul(left_side, right_side, precision=lax.Precision.HIGHEST)


def tmat(matrix):
    return jnp.swapaxes(matrix, -1, -2)


def invert_small(matrix):
    lower_factor = jnp.linalg.cholesky(matrix)
    identity = jnp.eye(matrix.shape[-1], dtype=matrix.dtype)
    lower_inverse = jax.scipy.linalg.solve_triangular(lower_factor, identity, lower=True)
    return matmul(lower_inverse.T, lower_inverse)


def sweep(matrix, span, pivot):
    column = matrix[:, span]
    scaled = matmul(column, pivot)
    matrix = matrix - matmul(scaled, column.T)
    scaled = scaled.at[span].set(-pivot)
    return matrix.at[:, span].set(scaled).at[span, :].set(scaled.T)


def lower_solve(lower_factor, rhs):
    return jax.scipy.linalg.solve_triangular(lower_factor, rhs, lower=True)


def expand_mask(couple, couple_mask):
    cell_count = couple.shape[0]
    mask_width = couple_mask.shape[1]
    shaped = couple.reshape(cell_count, mask_width, BLK, mask_width, BLK)
    return (shaped * couple_mask[:, :, None, :, None].astype(couple.dtype)).reshape(couple.shape)


def combine(left_seg, right_seg):
    p_a, q_a, r_a = left_seg
    p_b, q_b, r_b = right_seg
    surface = r_a.shape[-1]
    eye = jnp.eye(surface, dtype=r_a.dtype)
    root = jnp.linalg.cholesky(r_a)
    root_t = tmat(root)
    lp = matmul(root_t, p_b)
    reduced = eye - matmul(lp, root)
    root_reduced = jnp.linalg.cholesky(reduced)
    rhs = jnp.concatenate([matmul(root_t, q_b), matmul(lp, tmat(q_a))], axis=-1)
    solved = lower_solve(root_reduced, rhs)
    gram = matmul(tmat(solved), solved)
    r_c = r_b + gram[..., :surface, :surface]
    q_c = matmul(q_a, q_b) + gram[..., surface:, :surface]
    p_c = p_a + matmul(matmul(q_a, p_b), tmat(q_a)) + gram[..., surface:, surface:]
    return (p_c, q_c, r_c)


def self_energy(regrouped, derivative, pair_list):
    first_pick = jnp.take(regrouped, pair_list[:, 0], axis=0)
    second_pick = jnp.take(regrouped, pair_list[:, 1], axis=0)
    pair_count = pair_list.shape[0]
    listed = derivative.shape[0]
    first_pick = first_pick.reshape(pair_count, listed, BLK, BLK)
    second_pick = second_pick.reshape(pair_count, listed, BLK, BLK)
    coupling_mat = derivative.reshape(listed, BLK, BLK)
    high = lax.Precision.HIGHEST
    left_side = jnp.einsum("nij,pnjk->pnik", coupling_mat, first_pick, precision=high)
    left_side = jnp.einsum("pnik,nlk->pnil", left_side, coupling_mat, precision=high)
    result = jnp.einsum("pnil,pnml->npim", left_side, second_pick, precision=high)
    return result.reshape(listed, pair_count, BLK * BLK)


def on_device(
    ham_diag, couple, couple_mask, energies, lead_front, block_list, derivative, pair_list
):
    cell_count = lax.axis_size("cell")
    cell_index = lax.axis_index("cell")
    surface = couple.shape[1]
    size = ham_diag.shape[1]
    coupling = expand_mask(couple, couple_mask)[0]
    eye = jnp.eye(surface, dtype=jnp.float32)
    is_first = cell_index == 0
    is_last = cell_index == cell_count - 1

    lead_self = matmul(matmul(coupling, lead_front[0]), coupling.T)
    lead_self = jnp.where(is_first, lead_self, jnp.zeros_like(lead_self))
    shifted = ham_diag[0] - energies[0] * jnp.eye(size, dtype=jnp.float32)
    shifted = shifted.at[:surface, :surface].add(-lead_self)
    state = shifted
    for start in range(surface, size, surface):
        span = slice(start, start + surface)
        state = sweep(state, span, invert_small(state[span, span]))
    schur = state[:surface, :surface]
    schur_edge = state[:surface, -surface:]
    corner = invert_small(schur)
    leaf = (
        matmul(matmul(coupling.T, corner), coupling),
        -matmul(coupling.T, matmul(corner, schur_edge)),
        matmul(matmul(schur_edge.T, corner), schur_edge) - state[-surface:, -surface:],
    )
    prefix = leaf
    distance = 1
    while distance < cell_count:
        from_left = passed_along(prefix, "cell", distance)
        has_left = cell_index >= distance
        safe_left = (from_left[0], from_left[1], jnp.where(has_left, from_left[2], eye))
        joined = combine(safe_left, prefix)
        prefix = tuple(jnp.where(has_left, j, o) for j, o in zip(joined, prefix))
        distance *= 2

    front_before = passed_along(prefix[2], "cell", 1)
    left_self = matmul(matmul(coupling, front_before), coupling.T)
    left_self = jnp.where(is_first, jnp.zeros_like(left_self), left_self)
    first_span = slice(0, surface)
    green = -sweep(state, first_span, invert_small(schur - left_self))

    edge_rows = green[-surface:, :]
    step_b = matmul(coupling.T, green[:surface, -surface:])
    step_a = matmul(matmul(coupling.T, green[:surface, :surface]), coupling)
    distance = 1
    while distance < cell_count:
        far_a, far_b = passed_along((step_a, step_b), "cell", -distance)
        step_a = step_a + matmul(matmul(step_b, far_a), step_b.T)
        step_b = matmul(step_b, far_b)
        distance *= 2
    weights = passed_along(step_a, "cell", -1)
    weights = jnp.where(is_last, jnp.zeros_like(weights), weights)
    full = green + matmul(edge_rows.T, matmul(weights, edge_rows))

    local_density = jnp.diagonal(full)[None]
    block_count = size // BLK
    picked = full.reshape(block_count, BLK, block_count, BLK)[
        block_list[0, :, 0], :, block_list[0, :, 1], :
    ]
    picked = picked.reshape(1, block_list.shape[1], BLK * BLK)
    regrouped = lax.all_to_all(picked, "energy", split_axis=1, concat_axis=0, tiled=True)
    result = self_energy(regrouped, derivative[0], pair_list)
    return (local_density, result[None])


def solution(mesh):
    placed = (
        P("cell", None, None),
        P("cell", None, None),
        P("cell", None, None),
        P("energy"),
        P("energy", None, None),
        P("cell", None, None),
        P("cell", "energy", None),
        P(),
    )
    return jax.shard_map(
        on_device,
        mesh=mesh,
        in_specs=placed,
        out_specs=(P("energy", "cell"), P("cell", "energy", None, None)),
        check_vma=False,
    )
```

```python
import jax
import jax.numpy as jnp
from jax import lax
from jax.sharding import PartitionSpec as P

BLK = 64


def passed_along(value, axis, steps):
    count = lax.axis_size(axis)
    first, last = (max(0, -steps), min(count, count - steps))
    return lax.ppermute(value, axis, [(source, source + steps) for source in range(first, last)])


def matmul(left_side, right_side):
    return jnp.matmul(left_side, right_side, precision=lax.Precision.HIGHEST)


def tmat(matrix):
    return jnp.swapaxes(matrix, -1, -2)


def invert_small(matrix):
    lower_factor = jnp.linalg.cholesky(matrix)
    identity = jnp.eye(matrix.shape[-1], dtype=matrix.dtype)
    lower_inverse = jax.scipy.linalg.solve_triangular(lower_factor, identity, lower=True)
    return matmul(lower_inverse.T, lower_inverse)


def sweep(matrix, span, pivot):
    column = matrix[:, span]
    scaled = matmul(column, pivot)
    matrix = matrix - matmul(scaled, column.T)
    scaled = scaled.at[span].set(-pivot)
    return matrix.at[:, span].set(scaled).at[span, :].set(scaled.T)


def lower_solve(lower_factor, rhs):
    return jax.scipy.linalg.solve_triangular(lower_factor, rhs, lower=True)


def expand_mask(couple, couple_mask):
    cell_count = couple.shape[0]
    mask_width = couple_mask.shape[1]
    shaped = couple.reshape(cell_count, mask_width, BLK, mask_width, BLK)
    return (shaped * couple_mask[:, :, None, :, None].astype(couple.dtype)).reshape(couple.shape)


def combine(left_seg, right_seg):
    p_a, q_a, r_a = left_seg
    p_b, q_b, r_b = right_seg
    surface = r_a.shape[-1]
    eye = jnp.eye(surface, dtype=r_a.dtype)
    root = jnp.linalg.cholesky(r_a)
    root_t = tmat(root)
    lp = matmul(root_t, p_b)
    reduced = eye - matmul(lp, root)
    root_reduced = jnp.linalg.cholesky(reduced)
    rhs = jnp.concatenate([matmul(root_t, q_b), matmul(lp, tmat(q_a))], axis=-1)
    solved = lower_solve(root_reduced, rhs)
    gram = matmul(tmat(solved), solved)
    r_c = r_b + gram[..., :surface, :surface]
    q_c = matmul(q_a, q_b) + gram[..., surface:, :surface]
    p_c = p_a + matmul(matmul(q_a, p_b), tmat(q_a)) + gram[..., surface:, surface:]
    return (p_c, q_c, r_c)


def self_energy(regrouped, derivative, pair_list):
    energy_count = regrouped.shape[0]
    flat = regrouped.reshape(energy_count, -1)
    levels = jnp.arange(energy_count, dtype=pair_list.dtype)
    first_pick = matmul((pair_list[:, 0:1] == levels).astype(flat.dtype), flat)
    second_pick = matmul((pair_list[:, 1:2] == levels).astype(flat.dtype), flat)
    pair_count = pair_list.shape[0]
    listed = derivative.shape[0]
    first_pick = first_pick.reshape(pair_count, listed, BLK, BLK)
    second_pick = second_pick.reshape(pair_count, listed, BLK, BLK)
    coupling_mat = derivative.reshape(listed, BLK, BLK)
    high = lax.Precision.HIGHEST
    left_side = jnp.einsum("nij,pnjk->pnik", coupling_mat, first_pick, precision=high)
    left_side = jnp.einsum("pnik,nlk->pnil", left_side, coupling_mat, precision=high)
    result = jnp.einsum("pnil,pnml->npim", left_side, second_pick, precision=high)
    return result.reshape(listed, pair_count, BLK * BLK)


def on_device(
    ham_diag, couple, couple_mask, energies, lead_front, block_list, derivative, pair_list
):
    cell_count = lax.axis_size("cell")
    cell_index = lax.axis_index("cell")
    surface = couple.shape[1]
    size = ham_diag.shape[1]
    coupling = expand_mask(couple, couple_mask)[0]
    eye = jnp.eye(surface, dtype=jnp.float32)
    is_first = cell_index == 0
    is_last = cell_index == cell_count - 1

    lead_self = matmul(matmul(coupling, lead_front[0]), coupling.T)
    lead_self = jnp.where(is_first, lead_self, jnp.zeros_like(lead_self))
    shifted = ham_diag[0] - energies[0] * jnp.eye(size, dtype=jnp.float32)
    shifted = shifted.at[:surface, :surface].add(-lead_self)
    state = shifted
    for start in range(surface, size, surface):
        span = slice(start, start + surface)
        state = sweep(state, span, invert_small(state[span, span]))
    schur = state[:surface, :surface]
    schur_edge = state[:surface, -surface:]
    corner = invert_small(schur)
    leaf = (
        matmul(matmul(coupling.T, corner), coupling),
        -matmul(coupling.T, matmul(corner, schur_edge)),
        matmul(matmul(schur_edge.T, corner), schur_edge) - state[-surface:, -surface:],
    )
    prefix = leaf
    distance = 1
    while distance < cell_count:
        from_left = passed_along(prefix, "cell", distance)
        has_left = cell_index >= distance
        safe_left = (from_left[0], from_left[1], jnp.where(has_left, from_left[2], eye))
        joined = combine(safe_left, prefix)
        prefix = tuple(jnp.where(has_left, j, o) for j, o in zip(joined, prefix))
        distance *= 2

    front_before = passed_along(prefix[2], "cell", 1)
    left_self = matmul(matmul(coupling, front_before), coupling.T)
    left_self = jnp.where(is_first, jnp.zeros_like(left_self), left_self)
    first_span = slice(0, surface)
    green = -sweep(state, first_span, invert_small(schur - left_self))

    edge_rows = green[-surface:, :]
    step_b = matmul(coupling.T, green[:surface, -surface:])
    step_a = matmul(matmul(coupling.T, green[:surface, :surface]), coupling)
    distance = 1
    while distance < cell_count:
        far_a, far_b = passed_along((step_a, step_b), "cell", -distance)
        step_a = step_a + matmul(matmul(step_b, far_a), step_b.T)
        step_b = matmul(step_b, far_b)
        distance *= 2
    weights = passed_along(step_a, "cell", -1)
    weights = jnp.where(is_last, jnp.zeros_like(weights), weights)
    full = green + matmul(edge_rows.T, matmul(weights, edge_rows))

    local_density = jnp.diagonal(full)[None]
    block_count = size // BLK
    row_blocks = full.reshape(block_count, BLK, size)[block_list[0, :, 0]]
    orbital = jnp.arange(size, dtype=block_list.dtype)[None, :, None]
    within = jnp.arange(BLK, dtype=block_list.dtype)[None, None, :]
    column_pick = orbital == block_list[0, :, 1][:, None, None] * BLK + within
    picked = jnp.einsum(
        "bik,bkj->bij", row_blocks, column_pick.astype(full.dtype), precision=lax.Precision.HIGHEST
    )
    picked = picked.reshape(1, block_list.shape[1], BLK * BLK)
    regrouped = lax.all_to_all(picked, "energy", split_axis=1, concat_axis=0, tiled=True)
    result = self_energy(regrouped, derivative[0], pair_list)
    return (local_density, result[None])


def solution(mesh):
    placed = (
        P("cell", None, None),
        P("cell", None, None),
        P("cell", None, None),
        P("energy"),
        P("energy", None, None),
        P("cell", None, None),
        P("cell", "energy", None),
        P(),
    )
    return jax.shard_map(
        on_device,
        mesh=mesh,
        in_specs=placed,
        out_specs=(P("energy", "cell"), P("cell", "energy", None, None)),
        check_vma=False,
    )
```
